256 devices in a mesh: panel: 2 (over z_lo), wide: 32 (over y, z_hi, core), narrow: 4 (over x).
Axes of the slice: x: 4, y: 4, z: 8 (z_hi: 4, z_lo: 2; z = z_hi * 2 + z_lo), core: 2. Of those that a mesh axis runs over, the one named last changes fastest.
Arguments:
- heat_scalar: float32 [2, 64, 1536, 512], P('panel', None, 'wide', 'narrow'), may hold values from -6 to 6
- polar_flow_speed: bfloat16 [2, 64, 1536, 512], P('panel', None, 'wide', 'narrow'), may hold values from -4 to 4
- azimuthal_flow_speed: bfloat16 [2, 64, 1536, 512], P('panel', None, 'wide', 'narrow'), may hold values from -4 to 4
- conduction_coefficient: float32 [2, 64, 1536, 512], P('panel', None, 'wide', 'narrow'), may hold values from 0.01 to 0.1
- interpolant_anchor_position: int32 [2, 4, 32, 64], P('panel', 'narrow', 'wide'), may hold values from 0 to 6143
- interpolant_factors: float32 [2, 4, 32, 2, 64], P('panel', 'narrow', 'wide'), may hold values from 0 to 1
- boundary_source_slot: int32 [2, 4, 32, 352], P('panel', 'narrow', 'wide'), may hold values from -1 to 8191, as said below
Outputs:
- temperature_next: float32 [2, 64, 1536, 512], P('panel', None, 'wide', 'narrow')
The draws below stay inside these ranges and needn't reach their ends.
Inputs may be any that keep to these rules, and one draw needn't show every extreme that they name: `boundary_source_slot`: entries are d * 64 + e, naming entry e of the donor tile with wide index d // 4 and narrow index d % 4 of the other panel; exactly the rim cells that lie outside the panel carry such an entry, the others -1; each donor entry fills at most one cell, a tile's used entries are its first ones, every tile uses at most 64 entries and some tile exactly 64; all but at most one of the tiles that use any entry use 3 * 16 or more.
All inputs are finite; a program needn't handle non-finite values.
Results may differ from the reference program's by a relative error of at most 0.0003.
Values sent between devices are 32-bit elements; how exact they have to be, the bound alone decides.
No kernel may reach another device: no remote copies, remote signals or barrier semaphores. Data moves between devices by JAX's collectives and lax.ppermute only.
A program may use at most 128 MiB of HBM per device.

```python
import math
import jax
import jax.numpy as jnp
from jax import lax

SHELL_DEPTH_SIZE = 64
CT = 128
CP = 48
TILE_ROWS = 4
TILE_COLS = 32
POLAR_ANGLE_COUNT = 512
AZIMUTH_COUNT = 1536
CAP = 64
GS = 352


def cycle_sources(seed_key):
    tiles = TILE_ROWS * TILE_COLS
    cycle_length = 2 * (POLAR_ANGLE_COUNT + AZIMUTH_COUNT)
    key_order, key_counts, key_shift = jax.random.split(seed_key, 3)
    shift = jax.random.randint(key_shift, (), 0, cycle_length).astype(jnp.int32)
    position = jnp.arange(cycle_length, dtype=jnp.int32)
    beside_all = (position + shift) % cycle_length
    in_upper = beside_all < AZIMUTH_COUNT
    in_east = (beside_all >= AZIMUTH_COUNT) & (beside_all < AZIMUTH_COUNT + POLAR_ANGLE_COUNT)
    in_lower = (beside_all >= AZIMUTH_COUNT + POLAR_ANGLE_COUNT) & (beside_all < 2 * AZIMUTH_COUNT + POLAR_ANGLE_COUNT)
    east_row = beside_all - AZIMUTH_COUNT
    lower_col = AZIMUTH_COUNT - 1 - (beside_all - AZIMUTH_COUNT - POLAR_ANGLE_COUNT)
    west_row = POLAR_ANGLE_COUNT - 1 - (beside_all - 2 * AZIMUTH_COUNT - POLAR_ANGLE_COUNT)
    tile_row = jnp.where(in_upper, 0, jnp.where(in_east, east_row // CT, jnp.where(in_lower, TILE_ROWS - 1, west_row // CT)))
    tile_col = jnp.where(in_upper, beside_all // CP, jnp.where(in_east, TILE_COLS - 1, jnp.where(in_lower, lower_col // CP, 0)))
    slot_index = jnp.where(in_upper, beside_all % CP, jnp.where(in_east, 2 * CP + CT + east_row % CT, jnp.where(in_lower, CP + lower_col % CP, 2 * CP + west_row % CT)))
    far_tile = ((tile_col[0] + TILE_COLS // 2) % TILE_COLS * TILE_ROWS + tile_row[0]).astype(jnp.int32)
    same_tile = (tile_col[CAP] * TILE_ROWS + tile_row[CAP]).astype(jnp.int32)
    scores = jax.random.permutation(key_order, tiles).astype(jnp.int32)
    scores = scores.at[same_tile].set(-1).at[far_tile].set(-2)
    order = jnp.argsort(scores, stable=True).astype(jnp.int32)
    counts = jax.random.randint(key_counts, (tiles,), 3 * CAP // 4, CAP + 1).astype(jnp.int32)
    counts = counts.at[0].set(CAP)
    ends = jnp.cumsum(counts).astype(jnp.int32)
    starts = ends - counts
    place_number = jnp.searchsorted(ends, position, side='right').astype(jnp.int32)
    value = order[place_number] * CAP + position - starts[place_number]
    empty = jnp.full((TILE_ROWS, TILE_COLS, GS), -1, jnp.int32)
    return empty.at[tile_row, tile_col, slot_index].set(value.astype(jnp.int32))


def draw_boundary_source_slot(key, part):
    return jnp.stack([cycle_sources(jax.random.fold_in(key, 11)), cycle_sources(jax.random.fold_in(key, 12))])


def set_ends(array, stream_key, least, top_value):
    shape = array.shape
    index_at = [jax.random.randint(jax.random.fold_in(stream_key, axis), (), 0, shape[axis]) for axis in range(len(shape))]
    array = array.at[tuple(index_at)].set(least)
    longest = shape.index(max(shape))
    index_at[longest] = (index_at[longest] + 1) % shape[longest]
    return array.at[tuple(index_at)].set(top_value)


def level_of(rng, shape, cuts, least, largest):
    level, own = 1.0, jax.random.fold_in(rng, 6)
    for dim, shards_of in cuts:
        heights = jnp.exp(jax.random.uniform(jax.random.fold_in(own, dim), (shards_of,), jnp.float32, least / len(cuts), largest / len(cuts)))
        level = level * jnp.repeat(heights, shape[dim] // shards_of).reshape([-1 if axis == dim else 1 for axis in range(len(shape))])
    return level


def normal_values(rng, dims, spread, bound, cuts=(), held_as=jnp.bfloat16):
    factor_of = level_of(rng, dims, cuts, -0.22, 0.18) if cuts else 1.0
    values = jax.random.normal(rng, dims, jnp.float32) * spread * factor_of
    return jnp.minimum(jnp.maximum(values, -bound), bound).astype(held_as)


def setup_inputs(seed: int = 0) -> dict:
    splits = jax.random.split(jax.random.key(seed), 8)
    return {
        "heat_scalar": normal_values(splits[0], (2, SHELL_DEPTH_SIZE, AZIMUTH_COUNT, POLAR_ANGLE_COUNT), 1.0, 6.0, ((0, 2), (2, 32), (3, 4)), jnp.float32),
        "polar_flow_speed": normal_values(splits[1], (2, SHELL_DEPTH_SIZE, AZIMUTH_COUNT, POLAR_ANGLE_COUNT), 1.0, 4.0, ((0, 2), (2, 32), (3, 4))),
        "azimuthal_flow_speed": normal_values(splits[2], (2, SHELL_DEPTH_SIZE, AZIMUTH_COUNT, POLAR_ANGLE_COUNT), 1.0, 4.0, ((0, 2), (2, 32), (3, 4))),
        "conduction_coefficient": jnp.clip(jnp.exp(math.log(0.1) - 2.3025851 * jax.random.uniform(splits[3], (2, SHELL_DEPTH_SIZE, AZIMUTH_COUNT, POLAR_ANGLE_COUNT), jnp.float32) ** level_of(splits[3], (2, SHELL_DEPTH_SIZE, AZIMUTH_COUNT, POLAR_ANGLE_COUNT), ((0, 2), (2, 32), (3, 4)), -0.2, 0.2)), 0.01, 0.1),
        "interpolant_anchor_position": set_ends(jax.random.randint(splits[4], (2, TILE_ROWS, TILE_COLS, CAP), 0, CT * CP), jax.random.fold_in(splits[4], 1), 0, (CT * CP) - 1).astype(jnp.int32),
        "interpolant_factors": jnp.clip(1.0 * jax.random.uniform(splits[5], (2, TILE_ROWS, TILE_COLS, 2, CAP), jnp.float32) ** level_of(splits[5], (2, TILE_ROWS, TILE_COLS, 2, CAP), ((0, 2), (1, 4), (2, 32)), -0.2, 0.2), 0.0, 1.0),
        "boundary_source_slot": draw_boundary_source_slot(jax.random.fold_in(splits[7], 71), 0),
    }


TIME_INCREMENT = 0.5
MARGIN = 0.04


def inverse_metrics(level_values, row_values, total_rows, level_count):
    radius = 0.55 + 0.45 * (level_values + 0.5) / level_count
    angle_span = 0.5 * math.pi + 2.0 * MARGIN
    colatitude = 0.25 * math.pi - MARGIN + (row_values + 0.5) * angle_span / total_rows
    return 1.0 / radius, 1.0 / jnp.sin(colatitude)


def horizontal(extended, k_extended, speed_theta, speed_phi, radius_inv, sine_inv):
    centre = extended[..., 1:-1, 1:-1]
    upper_cell = extended[..., 1:-1, :-2]
    lower_cell = extended[..., 1:-1, 2:]
    west_cell = extended[..., :-2, 1:-1]
    east_cell = extended[..., 2:, 1:-1]
    k_centre = k_extended[..., 1:-1, 1:-1]
    k_upper = jnp.maximum(k_extended[..., 1:-1, :-2], k_centre)
    k_lower = jnp.maximum(k_extended[..., 1:-1, 2:], k_centre)
    k_west = jnp.maximum(k_extended[..., :-2, 1:-1], k_centre)
    k_east = jnp.maximum(k_extended[..., 2:, 1:-1], k_centre)
    transport = -0.5 * radius_inv * (speed_theta * (lower_cell - upper_cell) + speed_phi * sine_inv * (east_cell - west_cell))
    spread_terms = radius_inv * radius_inv * (k_lower * (lower_cell - centre) - k_upper * (centre - upper_cell) + sine_inv * sine_inv * (k_east * (east_cell - centre) - k_west * (centre - west_cell)))
    return transport + spread_terms


def radial(centre, k_centre):
    k_faces = 0.5 * (k_centre[1:] + k_centre[:-1])
    fluxes = k_faces * (centre[1:] - centre[:-1])
    zero_face = jnp.zeros_like(centre[:1])
    return jnp.concatenate([fluxes, zero_face], axis=0) - jnp.concatenate([zero_face, fluxes], axis=0)


def pad_field(values):
    return jnp.pad(values, ((0, 0), (1, 1), (1, 1)))


def donor_values(padded, cells, weights):
    col_in = cells // CT
    row_in = cells % CT
    tile_row = jnp.arange(TILE_ROWS, dtype=jnp.int32)[:, None, None]
    tile_col = jnp.arange(TILE_COLS, dtype=jnp.int32)[None, :, None]
    base_row = (tile_row * CT + row_in + 1).astype(jnp.int32)
    base_col = (tile_col * CP + col_in + 1).astype(jnp.int32)
    weight_a = weights[:, :, 0, :]
    weight_b = weights[:, :, 1, :]
    values = ((1.0 - weight_a) * (1.0 - weight_b) * padded[:, base_col, base_row]
              + weight_a * (1.0 - weight_b) * padded[:, base_col, base_row + 1]
              + (1.0 - weight_a) * weight_b * padded[:, base_col + 1, base_row]
              + weight_a * weight_b * padded[:, base_col + 1, base_row + 1])
    return jnp.transpose(values, (0, 2, 1, 3)).reshape(values.shape[0], -1)


def place_ghosts(padded, values, sources):
    slot_index = jnp.arange(GS, dtype=jnp.int32)
    in_upper = slot_index < CP
    in_lower = (slot_index >= CP) & (slot_index < 2 * CP)
    in_west = (slot_index >= 2 * CP) & (slot_index < 2 * CP + CT)
    row_local = jnp.where(in_upper, 0, jnp.where(in_lower, CT + 1, jnp.where(in_west, 1 + slot_index - 2 * CP, 1 + slot_index - 2 * CP - CT)))
    col_local = jnp.where(in_upper, 1 + slot_index, jnp.where(in_lower, 1 + slot_index - CP, jnp.where(in_west, 0, CP + 1)))
    tile_row = jnp.arange(TILE_ROWS, dtype=jnp.int32)[:, None, None]
    tile_col = jnp.arange(TILE_COLS, dtype=jnp.int32)[None, :, None]
    rows_global = (tile_row * CT + row_local[None, None, :]).astype(jnp.int32)
    cols_global = (tile_col * CP + col_local[None, None, :]).astype(jnp.int32)
    usable = sources >= 0
    received = jnp.take(values, jnp.clip(sources, 0).astype(jnp.int32), axis=1)
    received = jnp.where(usable[None], received, jnp.zeros_like(received))
    return padded.at[:, cols_global, rows_global].add(received)


def reference(heat_scalar, polar_flow_speed, azimuthal_flow_speed, conduction_coefficient, interpolant_anchor_position, interpolant_factors, boundary_source_slot):
    radius_inv, sine_inv = inverse_metrics(jnp.arange(SHELL_DEPTH_SIZE, dtype=jnp.float32), jnp.arange(POLAR_ANGLE_COUNT, dtype=jnp.float32), POLAR_ANGLE_COUNT, SHELL_DEPTH_SIZE)
    k_padded = [pad_field(conduction_coefficient[0]), pad_field(conduction_coefficient[1])]
    speeds_theta = [polar_flow_speed[0].astype(jnp.float32), polar_flow_speed[1].astype(jnp.float32)]
    speeds_phi = [azimuthal_flow_speed[0].astype(jnp.float32), azimuthal_flow_speed[1].astype(jnp.float32)]

    def evaluate_derivative(current_state):
        padded = [pad_field(current_state[0]), pad_field(current_state[1])]
        results = []
        for panel_id in range(2):
            other_id = 1 - panel_id
            values = donor_values(padded[other_id], interpolant_anchor_position[other_id], interpolant_factors[other_id])
            filled = place_ghosts(padded[panel_id], values, boundary_source_slot[panel_id])
            k_here = k_padded[panel_id]

            def level_rate(pieces):
                return horizontal(pieces[0], pieces[1], pieces[2], pieces[3], pieces[4], sine_inv)

            flat_part = lax.map(level_rate, (filled, k_here, speeds_theta[panel_id], speeds_phi[panel_id], radius_inv))
            results.append(flat_part + radial(filled[:, 1:-1, 1:-1], k_here[:, 1:-1, 1:-1]))
        return jnp.stack(results)

    predictor_state = heat_scalar + TIME_INCREMENT * evaluate_derivative(heat_scalar)
    return 0.5 * (heat_scalar + predictor_state + TIME_INCREMENT * evaluate_derivative(predictor_state))
```

```python
import math

import jax
import jax.numpy as jnp
from jax import lax
from jax.sharding import PartitionSpec as P

TIME_INCREMENT = 0.5
MARGIN = 0.04
HI = lax.Precision.HIGHEST


def shifted_in(shard, axis, dim, forward):
    peers, length = lax.axis_size(axis), shard.shape[dim]
    if forward:
        pairs = [(i, i + 1) for i in range(peers - 1)]
        piece = lax.index_in_dim(shard, length - 1, axis=dim, keepdims=False)
    else:
        pairs = [(i + 1, i) for i in range(peers - 1)]
        piece = lax.index_in_dim(shard, 0, axis=dim, keepdims=False)
    return lax.ppermute(piece, axis, pairs)


def halos(shard):
    west = shifted_in(shard, "wide", 1, True)
    east = shifted_in(shard, "wide", 1, False)
    upper = shifted_in(shard, "narrow", 2, True)
    lower = shifted_in(shard, "narrow", 2, False)
    return west, east, upper, lower


def corner_in(shard):
    wides, narrows = lax.axis_size("wide"), lax.axis_size("narrow")
    pairs = [
        ((w + 1) * narrows + n + 1, w * narrows + n)
        for w in range(wides - 1)
        for n in range(narrows - 1)
    ]
    return lax.ppermute(shard[:, 0, 0], ("wide", "narrow"), pairs)


def neighbours(x, west, east, upper, lower):
    up = jnp.concatenate([upper[:, :, None], x[:, :, :-1]], axis=2)
    down = jnp.concatenate([x[:, :, 1:], lower[:, :, None]], axis=2)
    left = jnp.concatenate([west[:, None, :], x[:, :-1, :]], axis=1)
    right = jnp.concatenate([x[:, 1:, :], east[:, None, :]], axis=1)
    return up, down, left, right


def inverse_metrics(level_values, row_values, total_rows, level_count):
    radius = 0.55 + 0.45 * (level_values + 0.5) / level_count
    angle_span = 0.5 * math.pi + 2.0 * MARGIN
    colatitude = 0.25 * math.pi - MARGIN + (row_values + 0.5) * angle_span / total_rows
    return (1.0 / radius, 1.0 / jnp.sin(colatitude))


def shards(
    heat_scalar,
    polar_flow_speed,
    azimuthal_flow_speed,
    conduction_coefficient,
    interpolant_anchor_position,
    interpolant_factors,
    boundary_source_slot,
):
    current_state = heat_scalar[0]
    level_count, col_count, row_count = current_state.shape
    speed_theta = polar_flow_speed[0].astype(jnp.float32)
    speed_phi = azimuthal_flow_speed[0].astype(jnp.float32)
    k_local = conduction_coefficient[0]
    row_global = lax.axis_index("narrow") * row_count + jnp.arange(row_count, dtype=jnp.int32)
    radius_inv, sine_inv = inverse_metrics(
        jnp.arange(level_count, dtype=jnp.float32),
        row_global.astype(jnp.float32),
        row_count * lax.axis_size("narrow"),
        level_count,
    )
    r3 = radius_inv[:, None, None]
    s3 = sine_inv[None, None, :]

    k_up, k_down, k_left, k_right = neighbours(k_local, *halos(k_local))
    k_up = jnp.maximum(k_up, k_local)
    k_down = jnp.maximum(k_down, k_local)
    k_left = jnp.maximum(k_left, k_local)
    k_right = jnp.maximum(k_right, k_local)
    k_faces = 0.5 * (k_local[1:] + k_local[:-1])

    r2 = radius_inv[:, None]
    coef_up = r2 * (0.5 * speed_theta[:, :, 0] + r2 * k_up[:, :, 0])
    coef_down = r2 * (-0.5 * speed_theta[:, :, -1] + r2 * k_down[:, :, -1])
    sw = sine_inv[None, :]
    coef_left = r2 * sw * (0.5 * speed_phi[:, 0, :] + r2 * sw * k_left[:, 0, :])
    coef_right = r2 * sw * (-0.5 * speed_phi[:, -1, :] + r2 * sw * k_right[:, -1, :])

    cells = interpolant_anchor_position[0, 0, 0]
    weight_a = interpolant_factors[0, 0, 0, 0]
    weight_b = interpolant_factors[0, 0, 0, 1]
    ext_rows = row_count + 1
    base = (cells // row_count) * ext_rows + cells % row_count
    flat = jnp.arange((col_count + 1) * ext_rows, dtype=jnp.int32)[:, None]
    weights = (
        jnp.where(flat == base[None], (1.0 - weight_a) * (1.0 - weight_b), 0.0)
        + jnp.where(flat == base[None] + 1, weight_a * (1.0 - weight_b), 0.0)
        + jnp.where(flat == base[None] + ext_rows, (1.0 - weight_a) * weight_b, 0.0)
        + jnp.where(flat == base[None] + ext_rows + 1, weight_a * weight_b, 0.0)
    )

    sources = boundary_source_slot[0, 0, 0]
    usable = (sources >= 0)[:, None]
    picks = jnp.clip(sources, 0)

    def ghosts_of(x, east, lower, corner):
        xe = jnp.concatenate([x, east[:, None, :]], axis=1)
        lower_e = jnp.concatenate([lower, corner[:, None]], axis=1)
        ext = jnp.concatenate([xe, lower_e[:, :, None]], axis=2)
        ext = ext.reshape(level_count, -1)
        values = jnp.einsum("ke,lk->el", weights, ext, precision=HI)
        crossed = lax.ppermute(values, "panel", [(0, 1), (1, 0)])
        table = lax.all_gather(crossed, ("wide", "narrow"), axis=0, tiled=True)
        got = jnp.take(table, picks, axis=0, mode="clip")
        got = jnp.where(usable, got, 0.0).T
        c = col_count
        return got[:, :c], got[:, c : 2 * c], got[:, 2 * c : 2 * c + row_count], got[:, 2 * c + row_count :]

    def bulk_rate(x, west, east, upper, lower):
        up, down, left, right = neighbours(x, west, east, upper, lower)
        transport = -0.5 * r3 * (speed_theta * (down - up) + speed_phi * s3 * (right - left))
        spread = (
            r3
            * r3
            * (
                k_down * (down - x)
                - k_up * (x - up)
                + s3 * s3 * (k_right * (right - x) - k_left * (x - left))
            )
        )
        fluxes = k_faces * (x[1:] - x[:-1])
        zero = jnp.zeros_like(x[:1])
        radial = jnp.concatenate([fluxes, zero], axis=0) - jnp.concatenate([zero, fluxes], axis=0)
        return transport + spread + radial

    def correction(g_up, g_down, g_left, g_right):
        c_up = coef_up * g_up
        c_down = coef_down * g_down
        c_left = coef_left * g_left
        c_right = coef_right * g_right
        rows = jnp.pad(c_up[:, :, None], ((0, 0), (0, 0), (0, row_count - 1))) + jnp.pad(
            c_down[:, :, None], ((0, 0), (0, 0), (row_count - 1, 0))
        )
        cols = jnp.pad(c_left[:, None, :], ((0, 0), (0, col_count - 1), (0, 0))) + jnp.pad(
            c_right[:, None, :], ((0, 0), (col_count - 1, 0), (0, 0))
        )
        return rows + cols

    def evaluate(x):
        west, east, upper, lower = halos(x)
        corner = corner_in(x)
        ghosts = ghosts_of(x, east, lower, corner)
        bulk = lax.optimization_barrier(bulk_rate(x, west, east, upper, lower))
        return bulk + correction(*ghosts)

    predictor_state = current_state + TIME_INCREMENT * evaluate(current_state)
    result = 0.5 * (
        current_state + predictor_state + TIME_INCREMENT * evaluate(predictor_state)
    )
    return result[None]


def solution(mesh):
    placed = (
        P("panel", None, "wide", "narrow"),
        P("panel", None, "wide", "narrow"),
        P("panel", None, "wide", "narrow"),
        P("panel", None, "wide", "narrow"),
        P("panel", "narrow", "wide", None),
        P("panel", "narrow", "wide", None, None),
        P("panel", "narrow", "wide", None),
    )
    return jax.shard_map(
        shards,
        mesh=mesh,
        in_specs=placed,
        out_specs=P("panel", None, "wide", "narrow"),
        check_vma=False,
    )
```

```python
import math

import jax
import jax.numpy as jnp
from jax import lax
from jax.sharding import PartitionSpec as P

TIME_INCREMENT = 0.5
MARGIN = 0.04
HI = lax.Precision.HIGHEST


def shifted_in(shard, axis, dim, forward):
    peers, length = lax.axis_size(axis), shard.shape[dim]
    if forward:
        pairs = [(i, i + 1) for i in range(peers - 1)]
        piece = lax.index_in_dim(shard, length - 1, axis=dim, keepdims=False)
    else:
        pairs = [(i + 1, i) for i in range(peers - 1)]
        piece = lax.index_in_dim(shard, 0, axis=dim, keepdims=False)
    return lax.ppermute(piece, axis, pairs)


def halos(shard):
    west = shifted_in(shard, "wide", 1, True)
    east = shifted_in(shard, "wide", 1, False)
    upper = shifted_in(shard, "narrow", 2, True)
    lower = shifted_in(shard, "narrow", 2, False)
    return west, east, upper, lower


def corner_in(shard):
    wides, narrows = lax.axis_size("wide"), lax.axis_size("narrow")
    pairs = [
        ((w + 1) * narrows + n + 1, w * narrows + n)
        for w in range(wides - 1)
        for n in range(narrows - 1)
    ]
    return lax.ppermute(shard[:, 0, 0], ("wide", "narrow"), pairs)


def neighbours(x, west, east, upper, lower):
    up = jnp.concatenate([upper[:, :, None], x[:, :, :-1]], axis=2)
    down = jnp.concatenate([x[:, :, 1:], lower[:, :, None]], axis=2)
    left = jnp.concatenate([west[:, None, :], x[:, :-1, :]], axis=1)
    right = jnp.concatenate([x[:, 1:, :], east[:, None, :]], axis=1)
    return up, down, left, right


def inverse_metrics(level_values, row_values, total_rows, level_count):
    radius = 0.55 + 0.45 * (level_values + 0.5) / level_count
    angle_span = 0.5 * math.pi + 2.0 * MARGIN
    colatitude = 0.25 * math.pi - MARGIN + (row_values + 0.5) * angle_span / total_rows
    return (1.0 / radius, 1.0 / jnp.sin(colatitude))


def shards(
    heat_scalar,
    polar_flow_speed,
    azimuthal_flow_speed,
    conduction_coefficient,
    interpolant_anchor_position,
    interpolant_factors,
    boundary_source_slot,
):
    current_state = heat_scalar[0]
    level_count, col_count, row_count = current_state.shape
    speed_theta = polar_flow_speed[0].astype(jnp.float32)
    speed_phi = azimuthal_flow_speed[0].astype(jnp.float32)
    k_local = conduction_coefficient[0]
    row_global = lax.axis_index("narrow") * row_count + jnp.arange(row_count, dtype=jnp.int32)
    radius_inv, sine_inv = inverse_metrics(
        jnp.arange(level_count, dtype=jnp.float32),
        row_global.astype(jnp.float32),
        row_count * lax.axis_size("narrow"),
        level_count,
    )
    r3 = radius_inv[:, None, None]
    s3 = sine_inv[None, None, :]

    k_up, k_down, k_left, k_right = neighbours(k_local, *halos(k_local))
    k_up = jnp.maximum(k_up, k_local)
    k_down = jnp.maximum(k_down, k_local)
    k_left = jnp.maximum(k_left, k_local)
    k_right = jnp.maximum(k_right, k_local)
    k_faces = 0.5 * (k_local[1:] + k_local[:-1])

    r2 = radius_inv[:, None]
    coef_up = r2 * (0.5 * speed_theta[:, :, 0] + r2 * k_up[:, :, 0])
    coef_down = r2 * (-0.5 * speed_theta[:, :, -1] + r2 * k_down[:, :, -1])
    sw = sine_inv[None, :]
    coef_left = r2 * sw * (0.5 * speed_phi[:, 0, :] + r2 * sw * k_left[:, 0, :])
    coef_right = r2 * sw * (-0.5 * speed_phi[:, -1, :] + r2 * sw * k_right[:, -1, :])

    cells = interpolant_anchor_position[0, 0, 0]
    weight_a = interpolant_factors[0, 0, 0, 0]
    weight_b = interpolant_factors[0, 0, 0, 1]
    col0 = (cells // row_count)[None]
    row0 = (cells % row_count)[None]
    rows_at = jnp.arange(row_count + 1, dtype=jnp.int32)[:, None]
    cols_at = jnp.arange(col_count + 1, dtype=jnp.int32)[:, None]
    w_rows = jnp.where(rows_at == row0, 1.0 - weight_a, 0.0) + jnp.where(
        rows_at == row0 + 1, weight_a, 0.0
    )
    w_cols = jnp.where(cols_at == col0, 1.0 - weight_b, 0.0) + jnp.where(
        cols_at == col0 + 1, weight_b, 0.0
    )

    sources = boundary_source_slot[0, 0, 0]
    usable = (sources >= 0)[:, None]
    capacity = cells.shape[0]
    narrows = lax.axis_size("narrow")
    donor_tile = jnp.clip(sources, 0) // capacity
    t_w = (donor_tile // narrows) ^ lax.axis_index("wide")
    t_n = (donor_tile % narrows) ^ lax.axis_index("narrow")
    position = ((t_w >> 1) & 3) + 4 * (t_n & 3) + 16 * ((t_w >> 3) & 3) + 64 * (t_w & 1)
    picks = position * capacity + jnp.clip(sources, 0) % capacity

    def gathered(values):
        wides = lax.axis_size("wide")
        parts = []
        for o in range(4):
            pairs = [(p * wides + w, (1 - p) * wides + (w ^ (o << 1))) for p in range(2) for w in range(wides)]
            parts.append(lax.ppermute(values, ("panel", "wide"), pairs))
        values = jnp.concatenate(parts, axis=0)
        for axis, shift, bits in (("narrow", 0, 2), ("wide", 3, 2), ("wide", 0, 1)):
            n = lax.axis_size(axis)
            parts = [values]
            for o in range(1, 1 << bits):
                parts.append(lax.ppermute(values, axis, [(i, i ^ (o << shift)) for i in range(n)]))
            values = jnp.concatenate(parts, axis=0)
        return values

    def ghosts_of(x, east, lower, corner):
        lc = level_count
        partial = jnp.dot(x.reshape(lc * col_count, row_count), w_rows[:row_count], precision=HI)
        values = jnp.sum(partial.reshape(lc, col_count, capacity) * w_cols[None, :col_count], axis=1)
        values = values + jnp.dot(east, w_rows[:row_count], precision=HI) * w_cols[col_count]
        values = values + jnp.dot(lower, w_cols[:col_count], precision=HI) * w_rows[row_count]
        values = values + corner[:, None] * (w_cols[col_count] * w_rows[row_count])[None]
        table = gathered(values.T)
        got = jnp.take(table, picks, axis=0, mode="clip")
        got = jnp.where(usable, got, 0.0).T
        c = col_count
        return got[:, :c], got[:, c : 2 * c], got[:, 2 * c : 2 * c + row_count], got[:, 2 * c + row_count :]

    def bulk_rate(x, west, east, upper, lower):
        up, down, left, right = neighbours(x, west, east, upper, lower)
        transport = -0.5 * r3 * (speed_theta * (down - up) + speed_phi * s3 * (right - left))
        spread = (
            r3
            * r3
            * (
                k_down * (down - x)
                - k_up * (x - up)
                + s3 * s3 * (k_right * (right - x) - k_left * (x - left))
            )
        )
        fluxes = k_faces * (x[1:] - x[:-1])
        zero = jnp.zeros_like(x[:1])
        radial = jnp.concatenate([fluxes, zero], axis=0) - jnp.concatenate([zero, fluxes], axis=0)
        return transport + spread + radial

    def correction(g_up, g_down, g_left, g_right):
        c_up = coef_up * g_up
        c_down = coef_down * g_down
        c_left = coef_left * g_left
        c_right = coef_right * g_right
        rows = jnp.pad(c_up[:, :, None], ((0, 0), (0, 0), (0, row_count - 1))) + jnp.pad(
            c_down[:, :, None], ((0, 0), (0, 0), (row_count - 1, 0))
        )
        cols = jnp.pad(c_left[:, None, :], ((0, 0), (0, col_count - 1), (0, 0))) + jnp.pad(
            c_right[:, None, :], ((0, 0), (col_count - 1, 0), (0, 0))
        )
        return rows + cols

    def evaluate(x):
        west, east, upper, lower = halos(x)
        corner = corner_in(x)
        ghosts = ghosts_of(x, east, lower, corner)
        bulk = lax.optimization_barrier(bulk_rate(x, west, east, upper, lower))
        return bulk + correction(*ghosts)

    predictor_state = current_state + TIME_INCREMENT * evaluate(current_state)
    result = 0.5 * (
        current_state + predictor_state + TIME_INCREMENT * evaluate(predictor_state)
    )
    return result[None]


def solution(mesh):
    placed = (
        P("panel", None, "wide", "narrow"),
        P("panel", None, "wide", "narrow"),
        P("panel", None, "wide", "narrow"),
        P("panel", None, "wide", "narrow"),
        P("panel", "narrow", "wide", None),
        P("panel", "narrow", "wide", None, None),
        P("panel", "narrow", "wide", None),
    )
    return jax.shard_map(
        shards,
        mesh=mesh,
        in_specs=placed,
        out_specs=P("panel", None, "wide", "narrow"),
        check_vma=False,
    )
```

```python
import math

import jax
import jax.numpy as jnp
from jax import lax
from jax.sharding import PartitionSpec as P

TIME_INCREMENT = 0.5
MARGIN = 0.04
HI = lax.Precision.HIGHEST


def shifted_in(shard, axis, dim, forward):
    peers, length = lax.axis_size(axis), shard.shape[dim]
    if forward:
        pairs = [(i, i + 1) for i in range(peers - 1)]
        piece = lax.index_in_dim(shard, length - 1, axis=dim, keepdims=False)
    else:
        pairs = [(i + 1, i) for i in range(peers - 1)]
        piece = lax.index_in_dim(shard, 0, axis=dim, keepdims=False)
    return lax.ppermute(piece, axis, pairs)


def halos(shard):
    west = shifted_in(shard, "wide", 1, True)
    east = shifted_in(shard, "wide", 1, False)
    upper = shifted_in(shard, "narrow", 2, True)
    lower = shifted_in(shard, "narrow", 2, False)
    return west, east, upper, lower


def corner_in(shard):
    wides, narrows = lax.axis_size("wide"), lax.axis_size("narrow")
    pairs = [
        ((w + 1) * narrows + n + 1, w * narrows + n)
        for w in range(wides - 1)
        for n in range(narrows - 1)
    ]
    return lax.ppermute(shard[:, 0, 0], ("wide", "narrow"), pairs)


def neighbours(x, west, east, upper, lower):
    up = jnp.concatenate([upper[:, :, None], x[:, :, :-1]], axis=2)
    down = jnp.concatenate([x[:, :, 1:], lower[:, :, None]], axis=2)
    left = jnp.concatenate([west[:, None, :], x[:, :-1, :]], axis=1)
    right = jnp.concatenate([x[:, 1:, :], east[:, None, :]], axis=1)
    return up, down, left, right


def inverse_metrics(level_values, row_values, total_rows, level_count):
    radius = 0.55 + 0.45 * (level_values + 0.5) / level_count
    angle_span = 0.5 * math.pi + 2.0 * MARGIN
    colatitude = 0.25 * math.pi - MARGIN + (row_values + 0.5) * angle_span / total_rows
    return (1.0 / radius, 1.0 / jnp.sin(colatitude))


def shards(
    heat_scalar,
    polar_flow_speed,
    azimuthal_flow_speed,
    conduction_coefficient,
    interpolant_anchor_position,
    interpolant_factors,
    boundary_source_slot,
):
    current_state = heat_scalar[0]
    level_count, col_count, row_count = current_state.shape
    speed_theta = polar_flow_speed[0].astype(jnp.float32)
    speed_phi = azimuthal_flow_speed[0].astype(jnp.float32)
    k_local = conduction_coefficient[0]
    row_global = lax.axis_index("narrow") * row_count + jnp.arange(row_count, dtype=jnp.int32)
    radius_inv, sine_inv = inverse_metrics(
        jnp.arange(level_count, dtype=jnp.float32),
        row_global.astype(jnp.float32),
        row_count * lax.axis_size("narrow"),
        level_count,
    )
    r3 = radius_inv[:, None, None]
    s3 = sine_inv[None, None, :]

    k_up, k_down, k_left, k_right = neighbours(k_local, *halos(k_local))
    k_up = jnp.maximum(k_up, k_local)
    k_down = jnp.maximum(k_down, k_local)
    k_left = jnp.maximum(k_left, k_local)
    k_right = jnp.maximum(k_right, k_local)
    k_faces = 0.5 * (k_local[1:] + k_local[:-1])

    r2 = radius_inv[:, None]
    coef_up = r2 * (0.5 * speed_theta[:, :, 0] + r2 * k_up[:, :, 0])
    coef_down = r2 * (-0.5 * speed_theta[:, :, -1] + r2 * k_down[:, :, -1])
    sw = sine_inv[None, :]
    coef_left = r2 * sw * (0.5 * speed_phi[:, 0, :] + r2 * sw * k_left[:, 0, :])
    coef_right = r2 * sw * (-0.5 * speed_phi[:, -1, :] + r2 * sw * k_right[:, -1, :])

    cells = interpolant_anchor_position[0, 0, 0]
    weight_a = interpolant_factors[0, 0, 0, 0]
    weight_b = interpolant_factors[0, 0, 0, 1]
    ext_rows = row_count + 1
    base = (cells // row_count) * ext_rows + cells % row_count
    flat = jnp.arange((col_count + 1) * ext_rows, dtype=jnp.int32)[:, None]
    weights = (
        jnp.where(flat == base[None], (1.0 - weight_a) * (1.0 - weight_b), 0.0)
        + jnp.where(flat == base[None] + 1, weight_a * (1.0 - weight_b), 0.0)
        + jnp.where(flat == base[None] + ext_rows, (1.0 - weight_a) * weight_b, 0.0)
        + jnp.where(flat == base[None] + ext_rows + 1, weight_a * weight_b, 0.0)
    )

    sources = boundary_source_slot[0, 0, 0]
    usable = (sources >= 0)[:, None]
    capacity = cells.shape[0]
    narrows = lax.axis_size("narrow")
    donor_tile = jnp.clip(sources, 0) // capacity
    t_w = (donor_tile // narrows) ^ lax.axis_index("wide")
    t_n = (donor_tile % narrows) ^ lax.axis_index("narrow")
    position = ((t_w >> 1) & 3) + 4 * (t_n & 3) + 16 * ((t_w >> 3) & 3) + 64 * (t_w & 1)
    picks = position * capacity + jnp.clip(sources, 0) % capacity

    def gathered(values):
        wides = lax.axis_size("wide")
        parts = []
        for o in range(4):
            pairs = [(p * wides + w, (1 - p) * wides + (w ^ (o << 1))) for p in range(2) for w in range(wides)]
            parts.append(lax.ppermute(values, ("panel", "wide"), pairs))
        values = jnp.concatenate(parts, axis=0)
        for axis, shift, bits in (("narrow", 0, 2), ("wide", 3, 2), ("wide", 0, 1)):
            n = lax.axis_size(axis)
            parts = [values]
            for o in range(1, 1 << bits):
                parts.append(lax.ppermute(values, axis, [(i, i ^ (o << shift)) for i in range(n)]))
            values = jnp.concatenate(parts, axis=0)
        return values

    def ghosts_of(x, east, lower, corner):
        xe = jnp.concatenate([x, east[:, None, :]], axis=1)
        lower_e = jnp.concatenate([lower, corner[:, None]], axis=1)
        ext = jnp.concatenate([xe, lower_e[:, :, None]], axis=2)
        ext = ext.reshape(level_count, -1)
        values = jnp.einsum("ke,lk->el", weights, ext, precision=HI)
        table = gathered(values)
        got = jnp.take(table, picks, axis=0, mode="clip")
        got = jnp.where(usable, got, 0.0).T
        c = col_count
        return got[:, :c], got[:, c : 2 * c], got[:, 2 * c : 2 * c + row_count], got[:, 2 * c + row_count :]

    def bulk_rate(x, west, east, upper, lower):
        up, down, left, right = neighbours(x, west, east, upper, lower)
        transport = -0.5 * r3 * (speed_theta * (down - up) + speed_phi * s3 * (right - left))
        spread = (
            r3
            * r3
            * (
                k_down * (down - x)
                - k_up * (x - up)
                + s3 * s3 * (k_right * (right - x) - k_left * (x - left))
            )
        )
        fluxes = k_faces * (x[1:] - x[:-1])
        zero = jnp.zeros_like(x[:1])
        radial = jnp.concatenate([fluxes, zero], axis=0) - jnp.concatenate([zero, fluxes], axis=0)
        return transport + spread + radial

    def correction(g_up, g_down, g_left, g_right):
        c_up = coef_up * g_up
        c_down = coef_down * g_down
        c_left = coef_left * g_left
        c_right = coef_right * g_right
        rows = jnp.pad(c_up[:, :, None], ((0, 0), (0, 0), (0, row_count - 1))) + jnp.pad(
            c_down[:, :, None], ((0, 0), (0, 0), (row_count - 1, 0))
        )
        cols = jnp.pad(c_left[:, None, :], ((0, 0), (0, col_count - 1), (0, 0))) + jnp.pad(
            c_right[:, None, :], ((0, 0), (col_count - 1, 0), (0, 0))
        )
        return rows + cols

    def evaluate(x):
        west, east, upper, lower = halos(x)
        corner = corner_in(x)
        ghosts = ghosts_of(x, east, lower, corner)
        bulk = lax.optimization_barrier(bulk_rate(x, west, east, upper, lower))
        return bulk + correction(*ghosts)

    predictor_state = current_state + TIME_INCREMENT * evaluate(current_state)
    result = 0.5 * (
        current_state + predictor_state + TIME_INCREMENT * evaluate(predictor_state)
    )
    return result[None]


def solution(mesh):
    placed = (
        P("panel", None, "wide", "narrow"),
        P("panel", None, "wide", "narrow"),
        P("panel", None, "wide", "narrow"),
        P("panel", None, "wide", "narrow"),
        P("panel", "narrow", "wide", None),
        P("panel", "narrow", "wide", None, None),
        P("panel", "narrow", "wide", None),
    )
    return jax.shard_map(
        shards,
        mesh=mesh,
        in_specs=placed,
        out_specs=P("panel", None, "wide", "narrow"),
        check_vma=False,
    )
```

```python
import math

import jax
import jax.numpy as jnp
from jax import lax
from jax.sharding import PartitionSpec as P

TIME_INCREMENT = 0.5
MARGIN = 0.04
HI = lax.Precision.HIGHEST


def shifted_in(shard, axis, dim, forward):
    peers, length = lax.axis_size(axis), shard.shape[dim]
    if forward:
        pairs = [(i, i + 1) for i in range(peers - 1)]
        piece = lax.index_in_dim(shard, length - 1, axis=dim, keepdims=False)
    else:
        pairs = [(i + 1, i) for i in range(peers - 1)]
        piece = lax.index_in_dim(shard, 0, axis=dim, keepdims=False)
    return lax.ppermute(piece, axis, pairs)


def halos(shard):
    west = shifted_in(shard, "wide", 1, True)
    east = shifted_in(shard, "wide", 1, False)
    upper = shifted_in(shard, "narrow", 2, True)
    lower = shifted_in(shard, "narrow", 2, False)
    return west, east, upper, lower


def corner_in(shard):
    wides, narrows = lax.axis_size("wide"), lax.axis_size("narrow")
    pairs = [
        ((w + 1) * narrows + n + 1, w * narrows + n)
        for w in range(wides - 1)
        for n in range(narrows - 1)
    ]
    return lax.ppermute(shard[:, 0, 0], ("wide", "narrow"), pairs)


def neighbours(x, west, east, upper, lower):
    up = jnp.concatenate([upper[:, :, None], x[:, :, :-1]], axis=2)
    down = jnp.concatenate([x[:, :, 1:], lower[:, :, None]], axis=2)
    left = jnp.concatenate([west[:, None, :], x[:, :-1, :]], axis=1)
    right = jnp.concatenate([x[:, 1:, :], east[:, None, :]], axis=1)
    return up, down, left, right


def inverse_metrics(level_values, row_values, total_rows, level_count):
    radius = 0.55 + 0.45 * (level_values + 0.5) / level_count
    angle_span = 0.5 * math.pi + 2.0 * MARGIN
    colatitude = 0.25 * math.pi - MARGIN + (row_values + 0.5) * angle_span / total_rows
    return (1.0 / radius, 1.0 / jnp.sin(colatitude))


def shards(
    heat_scalar,
    polar_flow_speed,
    azimuthal_flow_speed,
    conduction_coefficient,
    interpolant_anchor_position,
    interpolant_factors,
    boundary_source_slot,
):
    current_state = heat_scalar[0]
    level_count, col_count, row_count = current_state.shape
    speed_theta = polar_flow_speed[0].astype(jnp.float32)
    speed_phi = azimuthal_flow_speed[0].astype(jnp.float32)
    k_local = conduction_coefficient[0]
    row_global = lax.axis_index("narrow") * row_count + jnp.arange(row_count, dtype=jnp.int32)
    radius_inv, sine_inv = inverse_metrics(
        jnp.arange(level_count, dtype=jnp.float32),
        row_global.astype(jnp.float32),
        row_count * lax.axis_size("narrow"),
        level_count,
    )
    r3 = radius_inv[:, None, None]
    s3 = sine_inv[None, None, :]

    k_up, k_down, k_left, k_right = neighbours(k_local, *halos(k_local))
    k_up = jnp.maximum(k_up, k_local)
    k_down = jnp.maximum(k_down, k_local)
    k_left = jnp.maximum(k_left, k_local)
    k_right = jnp.maximum(k_right, k_local)
    k_faces = 0.5 * (k_local[1:] + k_local[:-1])

    r2 = radius_inv[:, None]
    coef_up = r2 * (0.5 * speed_theta[:, :, 0] + r2 * k_up[:, :, 0])
    coef_down = r2 * (-0.5 * speed_theta[:, :, -1] + r2 * k_down[:, :, -1])
    sw = sine_inv[None, :]
    coef_left = r2 * sw * (0.5 * speed_phi[:, 0, :] + r2 * sw * k_left[:, 0, :])
    coef_right = r2 * sw * (-0.5 * speed_phi[:, -1, :] + r2 * sw * k_right[:, -1, :])

    cells = interpolant_anchor_position[0, 0, 0]
    weight_a = interpolant_factors[0, 0, 0, 0]
    weight_b = interpolant_factors[0, 0, 0, 1]
    ext_rows = -(-(row_count + 1) // 8) * 8
    base = (cells // row_count) * ext_rows + cells % row_count
    flat = jnp.arange((col_count + 1) * ext_rows, dtype=jnp.int32)[:, None]
    weights = (
        jnp.where(flat == base[None], (1.0 - weight_a) * (1.0 - weight_b), 0.0)
        + jnp.where(flat == base[None] + 1, weight_a * (1.0 - weight_b), 0.0)
        + jnp.where(flat == base[None] + ext_rows, (1.0 - weight_a) * weight_b, 0.0)
        + jnp.where(flat == base[None] + ext_rows + 1, weight_a * weight_b, 0.0)
    )

    sources = boundary_source_slot[0, 0, 0]
    usable = (sources >= 0)[:, None]
    picks = jnp.clip(sources, 0)

    def ghosts_of(x, east, lower, corner):
        xe = jnp.concatenate([x, east[:, None, :]], axis=1)
        lower_e = jnp.concatenate([lower, corner[:, None]], axis=1)
        ext = jnp.concatenate([xe, lower_e[:, :, None]], axis=2)
        ext = jnp.pad(ext, ((0, 0), (0, 0), (0, ext_rows - row_count - 1)))
        ext = ext.reshape(level_count, -1)
        values = jnp.einsum("ke,lk->el", weights, ext, precision=HI)
        crossed = lax.ppermute(values, "panel", [(0, 1), (1, 0)])
        table = lax.all_gather(crossed, ("wide", "narrow"), axis=0, tiled=True)
        got = jnp.take(table, picks, axis=0, mode="clip")
        got = jnp.where(usable, got, 0.0).T
        c = col_count
        return got[:, :c], got[:, c : 2 * c], got[:, 2 * c : 2 * c + row_count], got[:, 2 * c + row_count :]

    def bulk_rate(x, west, east, upper, lower):
        up, down, left, right = neighbours(x, west, east, upper, lower)
        transport = -0.5 * r3 * (speed_theta * (down - up) + speed_phi * s3 * (right - left))
        spread = (
            r3
            * r3
            * (
                k_down * (down - x)
                - k_up * (x - up)
                + s3 * s3 * (k_right * (right - x) - k_left * (x - left))
            )
        )
        fluxes = k_faces * (x[1:] - x[:-1])
        zero = jnp.zeros_like(x[:1])
        radial = jnp.concatenate([fluxes, zero], axis=0) - jnp.concatenate([zero, fluxes], axis=0)
        return transport + spread + radial

    def correction(g_up, g_down, g_left, g_right):
        c_up = coef_up * g_up
        c_down = coef_down * g_down
        c_left = coef_left * g_left
        c_right = coef_right * g_right
        rows = jnp.pad(c_up[:, :, None], ((0, 0), (0, 0), (0, row_count - 1))) + jnp.pad(
            c_down[:, :, None], ((0, 0), (0, 0), (row_count - 1, 0))
        )
        cols = jnp.pad(c_left[:, None, :], ((0, 0), (0, col_count - 1), (0, 0))) + jnp.pad(
            c_right[:, None, :], ((0, 0), (col_count - 1, 0), (0, 0))
        )
        return rows + cols

    def evaluate(x):
        west, east, upper, lower = halos(x)
        corner = corner_in(x)
        ghosts = ghosts_of(x, east, lower, corner)
        bulk = lax.optimization_barrier(bulk_rate(x, west, east, upper, lower))
        return bulk + correction(*ghosts)

    predictor_state = current_state + TIME_INCREMENT * evaluate(current_state)
    result = 0.5 * (
        current_state + predictor_state + TIME_INCREMENT * evaluate(predictor_state)
    )
    return result[None]


def solution(mesh):
    placed = (
        P("panel", None, "wide", "narrow"),
        P("panel", None, "wide", "narrow"),
        P("panel", None, "wide", "narrow"),
        P("panel", None, "wide", "narrow"),
        P("panel", "narrow", "wide", None),
        P("panel", "narrow", "wide", None, None),
        P("panel", "narrow", "wide", None),
    )
    return jax.shard_map(
        shards,
        mesh=mesh,
        in_specs=placed,
        out_specs=P("panel", None, "wide", "narrow"),
        check_vma=False,
    )
```

```python
import math

import jax
import jax.numpy as jnp
from jax import lax
from jax.sharding import PartitionSpec as P

TIME_INCREMENT = 0.5
MARGIN = 0.04
HI = lax.Precision.HIGHEST


def shifted_in(shard, axis, dim, forward):
    peers, length = lax.axis_size(axis), shard.shape[dim]
    if forward:
        pairs = [(i, i + 1) for i in range(peers - 1)]
        piece = lax.index_in_dim(shard, length - 1, axis=dim, keepdims=False)
    else:
        pairs = [(i + 1, i) for i in range(peers - 1)]
        piece = lax.index_in_dim(shard, 0, axis=dim, keepdims=False)
    return lax.ppermute(piece, axis, pairs)


def halos(shard):
    west = shifted_in(shard, "wide", 1, True)
    east = shifted_in(shard, "wide", 1, False)
    upper = shifted_in(shard, "narrow", 2, True)
    lower = shifted_in(shard, "narrow", 2, False)
    return west, east, upper, lower


def corner_in(shard):
    wides, narrows = lax.axis_size("wide"), lax.axis_size("narrow")
    pairs = [
        ((w + 1) * narrows + n + 1, w * narrows + n)
        for w in range(wides - 1)
        for n in range(narrows - 1)
    ]
    return lax.ppermute(shard[:, 0, 0], ("wide", "narrow"), pairs)


def neighbours(x, west, east, upper, lower):
    up = jnp.concatenate([upper[:, :, None], x[:, :, :-1]], axis=2)
    down = jnp.concatenate([x[:, :, 1:], lower[:, :, None]], axis=2)
    left = jnp.concatenate([west[:, None, :], x[:, :-1, :]], axis=1)
    right = jnp.concatenate([x[:, 1:, :], east[:, None, :]], axis=1)
    return up, down, left, right


def inverse_metrics(level_values, row_values, total_rows, level_count):
    radius = 0.55 + 0.45 * (level_values + 0.5) / level_count
    angle_span = 0.5 * math.pi + 2.0 * MARGIN
    colatitude = 0.25 * math.pi - MARGIN + (row_values + 0.5) * angle_span / total_rows
    return (1.0 / radius, 1.0 / jnp.sin(colatitude))


def shards(
    heat_scalar,
    polar_flow_speed,
    azimuthal_flow_speed,
    conduction_coefficient,
    interpolant_anchor_position,
    interpolant_factors,
    boundary_source_slot,
):
    current_state = heat_scalar[0]
    level_count, col_count, row_count = current_state.shape
    speed_theta = polar_flow_speed[0].astype(jnp.float32)
    speed_phi = azimuthal_flow_speed[0].astype(jnp.float32)
    k_local = conduction_coefficient[0]
    row_global = lax.axis_index("narrow") * row_count + jnp.arange(row_count, dtype=jnp.int32)
    radius_inv, sine_inv = inverse_metrics(
        jnp.arange(level_count, dtype=jnp.float32),
        row_global.astype(jnp.float32),
        row_count * lax.axis_size("narrow"),
        level_count,
    )
    r3 = radius_inv[:, None, None]
    s3 = sine_inv[None, None, :]

    k_up, k_down, k_left, k_right = neighbours(k_local, *halos(k_local))
    k_up = jnp.maximum(k_up, k_local)
    k_down = jnp.maximum(k_down, k_local)
    k_left = jnp.maximum(k_left, k_local)
    k_right = jnp.maximum(k_right, k_local)
    k_faces = 0.5 * (k_local[1:] + k_local[:-1])

    r2 = radius_inv[:, None]
    coef_up = r2 * (0.5 * speed_theta[:, :, 0] + r2 * k_up[:, :, 0])
    coef_down = r2 * (-0.5 * speed_theta[:, :, -1] + r2 * k_down[:, :, -1])
    sw = sine_inv[None, :]
    coef_left = r2 * sw * (0.5 * speed_phi[:, 0, :] + r2 * sw * k_left[:, 0, :])
    coef_right = r2 * sw * (-0.5 * speed_phi[:, -1, :] + r2 * sw * k_right[:, -1, :])

    cells = interpolant_anchor_position[0, 0, 0]
    weight_a = interpolant_factors[0, 0, 0, 0]
    weight_b = interpolant_factors[0, 0, 0, 1]
    ext_rows = -(-(row_count + 1) // 8) * 8
    base = (cells // row_count) * ext_rows + cells % row_count
    flat = jnp.arange((col_count + 1) * ext_rows, dtype=jnp.int32)[:, None]
    weights = (
        jnp.where(flat == base[None], (1.0 - weight_a) * (1.0 - weight_b), 0.0)
        + jnp.where(flat == base[None] + 1, weight_a * (1.0 - weight_b), 0.0)
        + jnp.where(flat == base[None] + ext_rows, (1.0 - weight_a) * weight_b, 0.0)
        + jnp.where(flat == base[None] + ext_rows + 1, weight_a * weight_b, 0.0)
    )
    weights = lax.optimization_barrier(weights)

    sources = boundary_source_slot[0, 0, 0]
    usable = (sources >= 0)[:, None]
    picks = jnp.clip(sources, 0)

    def ghosts_of(x, east, lower, corner):
        xe = jnp.concatenate([x, east[:, None, :]], axis=1)
        lower_e = jnp.concatenate([lower, corner[:, None]], axis=1)
        ext = jnp.concatenate([xe, lower_e[:, :, None]], axis=2)
        ext = jnp.pad(ext, ((0, 0), (0, 0), (0, ext_rows - row_count - 1)))
        ext = ext.reshape(level_count, -1)
        values = jnp.einsum("ke,lk->el", weights, ext, precision=HI)
        crossed = lax.ppermute(values, "panel", [(0, 1), (1, 0)])
        table = lax.all_gather(crossed, ("wide", "narrow"), axis=0, tiled=True)
        got = jnp.take(table, picks, axis=0, mode="clip")
        got = jnp.where(usable, got, 0.0).T
        c = col_count
        return got[:, :c], got[:, c : 2 * c], got[:, 2 * c : 2 * c + row_count], got[:, 2 * c + row_count :]

    def bulk_rate(x, west, east, upper, lower):
        up, down, left, right = neighbours(x, west, east, upper, lower)
        transport = -0.5 * r3 * (speed_theta * (down - up) + speed_phi * s3 * (right - left))
        spread = (
            r3
            * r3
            * (
                k_down * (down - x)
                - k_up * (x - up)
                + s3 * s3 * (k_right * (right - x) - k_left * (x - left))
            )
        )
        fluxes = k_faces * (x[1:] - x[:-1])
        zero = jnp.zeros_like(x[:1])
        radial = jnp.concatenate([fluxes, zero], axis=0) - jnp.concatenate([zero, fluxes], axis=0)
        return transport + spread + radial

    def correction(g_up, g_down, g_left, g_right):
        c_up = coef_up * g_up
        c_down = coef_down * g_down
        c_left = coef_left * g_left
        c_right = coef_right * g_right
        rows = jnp.pad(c_up[:, :, None], ((0, 0), (0, 0), (0, row_count - 1))) + jnp.pad(
            c_down[:, :, None], ((0, 0), (0, 0), (row_count - 1, 0))
        )
        cols = jnp.pad(c_left[:, None, :], ((0, 0), (0, col_count - 1), (0, 0))) + jnp.pad(
            c_right[:, None, :], ((0, 0), (col_count - 1, 0), (0, 0))
        )
        return rows + cols

    def evaluate(x):
        west, east, upper, lower = halos(x)
        corner = corner_in(x)
        ghosts = ghosts_of(x, east, lower, corner)
        bulk = lax.optimization_barrier(bulk_rate(x, west, east, upper, lower))
        return bulk + correction(*ghosts)

    predictor_state = current_state + TIME_INCREMENT * evaluate(current_state)
    result = 0.5 * (
        current_state + predictor_state + TIME_INCREMENT * evaluate(predictor_state)
    )
    return result[None]


def solution(mesh):
    placed = (
        P("panel", None, "wide", "narrow"),
        P("panel", None, "wide", "narrow"),
        P("panel", None, "wide", "narrow"),
        P("panel", None, "wide", "narrow"),
        P("panel", "narrow", "wide", None),
        P("panel", "narrow", "wide", None, None),
        P("panel", "narrow", "wide", None),
    )
    return jax.shard_map(
        shards,
        mesh=mesh,
        in_specs=placed,
        out_specs=P("panel", None, "wide", "narrow"),
        check_vma=False,
    )
```
